256 devices in a mesh: gx: 16 (over z, x_hi), gy: 16 (over x_lo, y, core).
Axes of the slice: x: 4 (x_hi: 2, x_lo: 2; x = x_hi * 2 + x_lo), y: 4, z: 8, core: 2. Of those that a mesh axis runs over, the one named last changes fastest.
Arguments:
- adjoint_electric: float32 [3, 32, 2048, 512], P(None, 'gx', 'gy'), may hold values from -6 to 6
- adjoint_magnetic: float32 [3, 32, 2048, 512], P(None, 'gx', 'gy'), may hold values from -6 to 6
- second_electric: float32 [3, 32, 2048, 512], P(None, 'gx', 'gy'), may hold values from -6 to 6
- second_magnetic: float32 [3, 32, 2048, 512], P(None, 'gx', 'gy'), may hold values from -6 to 6
- saved_forward: bfloat16 [2, 3, 32, 2048, 512], P(None, None, 'gx', 'gy'), may hold values from -6 to 6
- saved_tangent: bfloat16 [2, 3, 32, 2048, 512], P(None, None, 'gx', 'gy'), may hold values from -6 to 6
- direction: float32 [32, 2048, 512], P('gx', 'gy'), may hold values from -6 to 6
- material: int32 [32, 2048, 512], P('gx', 'gy'), may hold values from 0 to 2
- source_mask: int32 [32, 2048, 512], P('gx', 'gy'), may hold values 0 or 1
Outputs:
- curvature: float32 [32, 2048, 512], P('gx', 'gy')
- updated_electric: float32 [3, 32, 2048, 512], P(None, 'gx', 'gy')
- updated_magnetic: float32 [3, 32, 2048, 512], P(None, 'gx', 'gy')
The draws below stay inside these ranges and needn't reach their ends.
Inputs may be any that keep to these rules, and one draw needn't show every extreme that they name: material 0 is absorber, 1 capping, 2 vacuum.
All inputs are finite; a program needn't handle non-finite values. No bound on the sum of `source_mask` on one device may be relied on, other than what follows from the above.
Results may differ from the reference program's by a relative error of at most 0.00045.
Values sent between devices are 32-bit elements; how exact they have to be, the bound alone decides.
No kernel may reach another device: no remote copies, remote signals or barrier semaphores. Data moves between devices by JAX's collectives and lax.ppermute only.
A program may use at most 192 MiB of HBM per device.

```python
import jax
import jax.numpy as jnp

STEPS = 2
NX = 32
NY = 2048
NZ = 512


def set_ends(array, own_key, smallest, largest):
    index_at = [jax.random.randint(jax.random.fold_in(own_key, axis), (), 0, length) for axis, length in enumerate(array.shape)]
    widest = array.shape.index(max(array.shape))
    beside = index_at[:widest] + [(index_at[widest] + 1) % array.shape[widest]] + index_at[widest + 1:]
    return array.at[tuple(index_at)].set(smallest).at[tuple(beside)].set(largest)


def levels(key, dims, cuts, low, top_value):
    def one(dim, parts):
        heights = jax.random.uniform(jax.random.fold_in(jax.random.fold_in(key, 6), dim), (parts,), jnp.float32, low / len(cuts), top_value / len(cuts))
        return jnp.repeat(jnp.exp(heights), dims[dim] // parts).reshape((-1,) + (1,) * (len(dims) - dim - 1))

    gain = one(*cuts[0])
    for cut in cuts[1:]:
        gain = gain * one(*cut)
    return gain


def bell_draw(rng, extent, spread, most, pieces=(), held_as=jnp.bfloat16):
    result = spread * jax.random.normal(rng, extent, jnp.float32)
    if pieces:
        result = result * levels(rng, extent, pieces, -0.22, 0.18)
    return jnp.clip(result, -most, most).astype(held_as)


def setup_inputs(seed: int = 0) -> dict:
    seeds = jax.random.split(jax.random.key(seed), 10)
    return {
        "adjoint_electric": bell_draw(seeds[0], (3, NX, NY, NZ), 1.0, 6.0, ((1, 16), (2, 16)), jnp.float32),
        "adjoint_magnetic": bell_draw(seeds[1], (3, NX, NY, NZ), 1.0, 6.0, ((1, 16), (2, 16)), jnp.float32),
        "second_electric": bell_draw(seeds[2], (3, NX, NY, NZ), 1.0, 6.0, ((1, 16), (2, 16)), jnp.float32),
        "second_magnetic": bell_draw(seeds[3], (3, NX, NY, NZ), 1.0, 6.0, ((1, 16), (2, 16)), jnp.float32),
        "saved_forward": bell_draw(seeds[4], (STEPS, 3, NX, NY, NZ), 1.0, 6.0, ((2, 16), (3, 16))),
        "saved_tangent": bell_draw(seeds[5], (STEPS, 3, NX, NY, NZ), 1.0, 6.0, ((2, 16), (3, 16))),
        "direction": bell_draw(seeds[6], (NX, NY, NZ), 1.0, 6.0, ((0, 16), (1, 16)), jnp.float32),
        "material": set_ends(jax.random.randint(seeds[7], (NX, NY, NZ), 0, 3), jax.random.fold_in(seeds[7], 1), 0, 2).astype(jnp.int32),
        "source_mask": set_ends((jax.random.randint(seeds[8], (NX, NY, NZ), 0, 4) < 1).astype(jnp.int32), jax.random.fold_in(seeds[8], 1), 0, 1),
    }


TIME_STEP = 0.5


def behind_x(field):
    return field - jnp.roll(field, 1, axis=0)


def behind_y(field):
    return field - jnp.roll(field, 1, axis=1)


def behind_z(field):
    return field - jnp.pad(field[:, :, :-1], ((0, 0), (0, 0), (1, 0)))


def ahead_x(field):
    return jnp.roll(field, -1, axis=0) - field


def ahead_y(field):
    return jnp.roll(field, -1, axis=1) - field


def ahead_z(field):
    return jnp.pad(field[:, :, 1:], ((0, 0), (0, 0), (0, 1))) - field


def curl_behind(field):
    return jnp.stack([behind_y(field[2]) - behind_z(field[1]),
                      behind_z(field[0]) - behind_x(field[2]),
                      behind_x(field[1]) - behind_y(field[0])])


def curl_ahead(field):
    return jnp.stack([ahead_y(field[2]) - ahead_z(field[1]),
                      ahead_z(field[0]) - ahead_x(field[2]),
                      ahead_x(field[1]) - ahead_y(field[0])])


def reference(adjoint_electric, adjoint_magnetic, second_electric, second_magnetic, saved_forward, saved_tangent, direction, material, source_mask):
    permittivity = jnp.where(material == 0, jnp.float32(2.6), jnp.where(material == 1, jnp.float32(1.8), jnp.float32(1.0)))
    coefficient = TIME_STEP / permittivity
    slope = -TIME_STEP * direction / (permittivity * permittivity)
    source = source_mask.astype(jnp.float32)
    curvature = jnp.zeros(direction.shape, jnp.float32)
    for section in reversed(range(STEPS)):
        forward = saved_forward[section].astype(jnp.float32)
        tangent = saved_tangent[section].astype(jnp.float32)
        adjoint_magnetic = adjoint_magnetic + TIME_STEP * curl_behind(coefficient * adjoint_electric)
        second_magnetic = second_magnetic + TIME_STEP * curl_behind(coefficient * second_electric + slope * adjoint_electric)
        adjoint_electric = adjoint_electric - TIME_STEP * curl_ahead(adjoint_magnetic) + source * forward
        second_electric = second_electric - TIME_STEP * curl_ahead(second_magnetic) + source * tangent
        curvature = curvature - (TIME_STEP / (permittivity * permittivity)) * jnp.sum(tangent * adjoint_electric + forward * second_electric, axis=0) \
            + (2.0 * TIME_STEP * direction / (permittivity * permittivity * permittivity)) * jnp.sum(forward * adjoint_electric, axis=0)
    return curvature, second_electric, second_magnetic
```

```python
import jax
import jax.numpy as jnp
from jax import lax
from jax.sharding import PartitionSpec as P


TIME_STEP = 0.5


def from_behind(block, axis, distance):
    devices = range(lax.axis_size(axis))
    route = [((i - distance) % len(devices), i) for i in devices]
    return lax.ppermute(block, axis, route)


def back_y(f, row):
    return f - jnp.concatenate([row[None], f[:-1]], axis=0)


def back_z(f):
    return f - jnp.pad(f[:, :-1], ((0, 0), (1, 0)))


def ahead_y(f, row):
    return jnp.concatenate([f[1:], row[None]], axis=0) - f


def ahead_z(f):
    return jnp.pad(f[:, 1:], ((0, 0), (0, 1))) - f


def magnetic_plane(h, w, prev, rows):
    bx2 = w[2] if prev is None else w[2] - prev[2]
    bx1 = w[1] if prev is None else w[1] - prev[1]
    return jnp.stack(
        [
            h[0] + TIME_STEP * (back_y(w[2], rows[1]) - back_z(w[1])),
            h[1] + TIME_STEP * (back_z(w[0]) - bx2),
            h[2] + TIME_STEP * (bx1 - back_y(w[0], rows[0])),
        ]
    )


def electric_plane(e, h, nxt, rows, add):
    return jnp.stack(
        [
            e[0] - TIME_STEP * (ahead_y(h[2], rows[1]) - ahead_z(h[1])) + add[0],
            e[1] - TIME_STEP * (ahead_z(h[0]) - (nxt[1] - h[2])) + add[1],
            e[2] - TIME_STEP * ((nxt[0] - h[1]) - ahead_y(h[0], rows[0])) + add[2],
        ]
    )


def local(
    adjoint_electric,
    adjoint_magnetic,
    second_electric,
    second_magnetic,
    saved_forward,
    saved_tangent,
    direction,
    material,
    source_mask,
):
    planes = adjoint_electric.shape[1]
    permittivity = jnp.where(
        material == 0,
        jnp.float32(2.6),
        jnp.where(material == 1, jnp.float32(1.8), jnp.float32(1.0)),
    )
    coefficient = TIME_STEP / permittivity
    slope = -TIME_STEP * direction / (permittivity * permittivity)
    source = source_mask.astype(jnp.float32)
    first_weight = TIME_STEP / (permittivity * permittivity)
    second_weight = 2.0 * TIME_STEP * direction / (permittivity * permittivity * permittivity)

    ea = [adjoint_electric[:, p] for p in range(planes)]
    ha = [adjoint_magnetic[:, p] for p in range(planes)]
    es = [second_electric[:, p] for p in range(planes)]
    hs = [second_magnetic[:, p] for p in range(planes)]
    coef = [coefficient[p] for p in range(planes)]
    slo = [slope[p] for p in range(planes)]
    src = [source[p] for p in range(planes)]
    fw1 = [first_weight[p] for p in range(planes)]
    fw2 = [second_weight[p] for p in range(planes)]
    curvature = [None] * planes

    total_steps = saved_forward.shape[0]
    for section in reversed(range(total_steps)):
      forward = [saved_forward[section][:, p].astype(jnp.float32) for p in range(planes)]
      tangent = [saved_tangent[section][:, p].astype(jnp.float32) for p in range(planes)]
      wa = [coef[p] * ea[p] for p in range(planes)]
      ws = [coef[p] * es[p] + slo[p] * ea[p] for p in range(planes)]
      last = planes - 1
      edge_x = jnp.stack([wa[last][1], wa[last][2], ws[last][1], ws[last][2]])
      before_x = from_behind(edge_x, "gx", 1)
      edge_y = jnp.stack([jnp.stack([wa[p][0, -1], wa[p][2, -1], ws[p][0, -1], ws[p][2, -1]]) for p in range(planes)])
      before_y = from_behind(edge_y, "gy", 1)

      ha_new = [None] * planes
      hs_new = [None] * planes
      ha_new[0] = magnetic_plane(ha[0], wa[0], None, before_y[0, 0:2])
      hs_new[0] = magnetic_plane(hs[0], ws[0], None, before_y[0, 2:4])
      front_x = jnp.stack([ha_new[0][1], ha_new[0][2], hs_new[0][1], hs_new[0][2]])
      ha_new[0], hs_new[0], front_x = lax.optimization_barrier((ha_new[0], hs_new[0], front_x))
      after_x = from_behind(front_x, "gx", -1)
      for p in range(1, planes):
          ha_new[p] = magnetic_plane(ha[p], wa[p], wa[p - 1], before_y[p, 0:2])
          hs_new[p] = magnetic_plane(hs[p], ws[p], ws[p - 1], before_y[p, 2:4])
      ha_new[0] = jnp.stack(
          [ha_new[0][0], ha_new[0][1] + TIME_STEP * before_x[1], ha_new[0][2] - TIME_STEP * before_x[0]]
      )
      hs_new[0] = jnp.stack(
          [hs_new[0][0], hs_new[0][1] + TIME_STEP * before_x[3], hs_new[0][2] - TIME_STEP * before_x[2]]
      )
      ha, hs = ha_new, hs_new
      front_y = jnp.stack(
          [jnp.stack([ha[p][0, 0], ha[p][2, 0], hs[p][0, 0], hs[p][2, 0]]) for p in range(planes)]
      )
      after_y = from_behind(front_y, "gy", -1)
      right_a = jnp.stack([after_x[0] + TIME_STEP * edge_x[1], after_x[1] - TIME_STEP * edge_x[0]])
      right_s = jnp.stack([after_x[2] + TIME_STEP * edge_x[3], after_x[3] - TIME_STEP * edge_x[2]])

      ea_new = [None] * planes
      es_new = [None] * planes
      for p in range(planes):
          nxt_a = right_a if p == last else ha[p + 1][1:3]
          nxt_s = right_s if p == last else hs[p + 1][1:3]
          ea_new[p] = electric_plane(ea[p], ha[p], nxt_a, after_y[p, 0:2], src[p] * forward[p])
          es_new[p] = electric_plane(es[p], hs[p], nxt_s, after_y[p, 2:4], src[p] * tangent[p])
      ea, es = ea_new, es_new
      for p in range(planes):
          term = -fw1[p] * jnp.sum(tangent[p] * ea[p] + forward[p] * es[p], axis=0) + fw2[p] * jnp.sum(
              forward[p] * ea[p], axis=0
          )
          curvature[p] = term if curvature[p] is None else curvature[p] + term
    return (
        jnp.stack(curvature),
        jnp.stack(es, axis=1),
        jnp.stack(hs, axis=1),
    )


def solution(mesh):
    in_specs = (
        P(None, "gx", "gy", None),
        P(None, "gx", "gy", None),
        P(None, "gx", "gy", None),
        P(None, "gx", "gy", None),
        P(None, None, "gx", "gy", None),
        P(None, None, "gx", "gy", None),
        P("gx", "gy", None),
        P("gx", "gy", None),
        P("gx", "gy", None),
    )
    out_specs = (P("gx", "gy", None), P(None, "gx", "gy", None), P(None, "gx", "gy", None))
    return jax.shard_map(local, mesh=mesh, in_specs=in_specs, out_specs=out_specs, check_vma=False)
```

```python
import jax
import jax.numpy as jnp
from jax import lax
from jax.sharding import PartitionSpec as P


TIME_STEP = 0.5


def from_behind(block, axis, distance):
    devices = range(lax.axis_size(axis))
    route = [((i - distance) % len(devices), i) for i in devices]
    return lax.ppermute(block, axis, route)


def back_y(f, row):
    return f - jnp.concatenate([row[None], f[:-1]], axis=0)


def back_z(f):
    return f - jnp.pad(f[:, :-1], ((0, 0), (1, 0)))


def ahead_y(f, row):
    return jnp.concatenate([f[1:], row[None]], axis=0) - f


def ahead_z(f):
    return jnp.pad(f[:, 1:], ((0, 0), (0, 1))) - f


def magnetic_plane(h, w, prev, rows):
    bx2 = w[2] if prev is None else w[2] - prev[2]
    bx1 = w[1] if prev is None else w[1] - prev[1]
    return jnp.stack(
        [
            h[0] + TIME_STEP * (back_y(w[2], rows[1]) - back_z(w[1])),
            h[1] + TIME_STEP * (back_z(w[0]) - bx2),
            h[2] + TIME_STEP * (bx1 - back_y(w[0], rows[0])),
        ]
    )


def electric_plane(e, h, nxt, rows, add):
    return jnp.stack(
        [
            e[0] - TIME_STEP * (ahead_y(h[2], rows[1]) - ahead_z(h[1])) + add[0],
            e[1] - TIME_STEP * (ahead_z(h[0]) - (nxt[1] - h[2])) + add[1],
            e[2] - TIME_STEP * ((nxt[0] - h[1]) - ahead_y(h[0], rows[0])) + add[2],
        ]
    )


def local(
    adjoint_electric,
    adjoint_magnetic,
    second_electric,
    second_magnetic,
    saved_forward,
    saved_tangent,
    direction,
    material,
    source_mask,
):
    planes = adjoint_electric.shape[1]
    permittivity = jnp.where(
        material == 0,
        jnp.float32(2.6),
        jnp.where(material == 1, jnp.float32(1.8), jnp.float32(1.0)),
    )
    coefficient = TIME_STEP / permittivity
    slope = -TIME_STEP * direction / (permittivity * permittivity)
    source = source_mask.astype(jnp.float32)
    first_weight = TIME_STEP / (permittivity * permittivity)
    second_weight = 2.0 * TIME_STEP * direction / (permittivity * permittivity * permittivity)

    ea = [adjoint_electric[:, p] for p in range(planes)]
    ha = [adjoint_magnetic[:, p] for p in range(planes)]
    es = [second_electric[:, p] for p in range(planes)]
    hs = [second_magnetic[:, p] for p in range(planes)]
    coef = [coefficient[p] for p in range(planes)]
    slo = [slope[p] for p in range(planes)]
    src = [source[p] for p in range(planes)]
    fw1 = [first_weight[p] for p in range(planes)]
    fw2 = [second_weight[p] for p in range(planes)]
    curvature = [None] * planes

    total_steps = saved_forward.shape[0]
    for section in reversed(range(total_steps)):
      forward = [saved_forward[section][:, p].astype(jnp.float32) for p in range(planes)]
      tangent = [saved_tangent[section][:, p].astype(jnp.float32) for p in range(planes)]
      wa = [coef[p] * ea[p] for p in range(planes)]
      ws = [coef[p] * es[p] + slo[p] * ea[p] for p in range(planes)]
      last = planes - 1
      edge_x = jnp.stack([wa[last][1], wa[last][2], ws[last][1], ws[last][2]])
      before_x = from_behind(edge_x, "gx", 1)
      edge_y = jnp.stack([jnp.stack([wa[p][0, -1], wa[p][2, -1], ws[p][0, -1], ws[p][2, -1]]) for p in range(planes)])
      before_y = from_behind(edge_y, "gy", 1)

      ha_new = [None] * planes
      hs_new = [None] * planes
      ha_new[0] = magnetic_plane(ha[0], wa[0], None, before_y[0, 0:2])
      hs_new[0] = magnetic_plane(hs[0], ws[0], None, before_y[0, 2:4])
      front_x = jnp.stack([ha_new[0][1], ha_new[0][2], hs_new[0][1], hs_new[0][2]])
      ha_new[0], hs_new[0], front_x = lax.optimization_barrier((ha_new[0], hs_new[0], front_x))
      after_x = from_behind(front_x, "gx", -1)
      for p in range(1, planes):
          ha_new[p] = magnetic_plane(ha[p], wa[p], wa[p - 1], before_y[p, 0:2])
          hs_new[p] = magnetic_plane(hs[p], ws[p], ws[p - 1], before_y[p, 2:4])
      ha_new[0] = jnp.stack(
          [ha_new[0][0], ha_new[0][1] + TIME_STEP * before_x[1], ha_new[0][2] - TIME_STEP * before_x[0]]
      )
      hs_new[0] = jnp.stack(
          [hs_new[0][0], hs_new[0][1] + TIME_STEP * before_x[3], hs_new[0][2] - TIME_STEP * before_x[2]]
      )
      ha, hs = lax.optimization_barrier((ha_new, hs_new))
      front_y = jnp.stack([jnp.stack([ha[p][0, 0], ha[p][2, 0], hs[p][0, 0], hs[p][2, 0]]) for p in range(planes)])
      after_y = from_behind(front_y, "gy", -1)
      right_a = jnp.stack([after_x[0] + TIME_STEP * edge_x[1], after_x[1] - TIME_STEP * edge_x[0]])
      right_s = jnp.stack([after_x[2] + TIME_STEP * edge_x[3], after_x[3] - TIME_STEP * edge_x[2]])

      ea_new = [None] * planes
      es_new = [None] * planes
      for p in range(planes):
          nxt_a = right_a if p == last else ha[p + 1][1:3]
          nxt_s = right_s if p == last else hs[p + 1][1:3]
          ea_new[p] = electric_plane(ea[p], ha[p], nxt_a, after_y[p, 0:2], src[p] * forward[p])
          es_new[p] = electric_plane(es[p], hs[p], nxt_s, after_y[p, 2:4], src[p] * tangent[p])
      ea, es = ea_new, es_new
      for p in range(planes):
          term = -fw1[p] * jnp.sum(tangent[p] * ea[p] + forward[p] * es[p], axis=0) + fw2[p] * jnp.sum(
              forward[p] * ea[p], axis=0
          )
          curvature[p] = term if curvature[p] is None else curvature[p] + term
    return (
        jnp.stack(curvature),
        jnp.stack(es, axis=1),
        jnp.stack(hs, axis=1),
    )


def solution(mesh):
    in_specs = (
        P(None, "gx", "gy", None),
        P(None, "gx", "gy", None),
        P(None, "gx", "gy", None),
        P(None, "gx", "gy", None),
        P(None, None, "gx", "gy", None),
        P(None, None, "gx", "gy", None),
        P("gx", "gy", None),
        P("gx", "gy", None),
        P("gx", "gy", None),
    )
    out_specs = (P("gx", "gy", None), P(None, "gx", "gy", None), P(None, "gx", "gy", None))
    return jax.shard_map(local, mesh=mesh, in_specs=in_specs, out_specs=out_specs, check_vma=False)
```

```python
import jax
import jax.numpy as jnp
from jax import lax
from jax.sharding import PartitionSpec as P


TIME_STEP = 0.5


def from_behind(block, axis, distance):
    devices = range(lax.axis_size(axis))
    route = [((i - distance) % len(devices), i) for i in devices]
    return lax.ppermute(block, axis, route)


def diagonal_route():
    nx, ny = lax.axis_size("gx"), lax.axis_size("gy")
    return [(i * ny + j, ((i - 1) % nx) * ny + (j + 1) % ny) for i in range(nx) for j in range(ny)]


def add_row0(f, row):
    return jnp.concatenate([(f[0] + row)[None], f[1:]], axis=0)


def back_y(f, row):
    return f - jnp.concatenate([row[None], f[:-1]], axis=0)


def back_z(f):
    return f - jnp.pad(f[:, :-1], ((0, 0), (1, 0)))


def ahead_y(f, row):
    return jnp.concatenate([f[1:], row[None]], axis=0) - f


def ahead_z(f):
    return jnp.pad(f[:, 1:], ((0, 0), (0, 1))) - f


def magnetic_plane(h, w, prev, rows):
    bx2 = w[2] if prev is None else w[2] - prev[2]
    bx1 = w[1] if prev is None else w[1] - prev[1]
    return jnp.stack(
        [
            h[0] + TIME_STEP * (back_y(w[2], rows[1]) - back_z(w[1])),
            h[1] + TIME_STEP * (back_z(w[0]) - bx2),
            h[2] + TIME_STEP * (bx1 - back_y(w[0], rows[0])),
        ]
    )


def electric_plane(e, h, nxt, rows, add):
    return jnp.stack(
        [
            e[0] - TIME_STEP * (ahead_y(h[2], rows[1]) - ahead_z(h[1])) + add[0],
            e[1] - TIME_STEP * (ahead_z(h[0]) - (nxt[1] - h[2])) + add[1],
            e[2] - TIME_STEP * ((nxt[0] - h[1]) - ahead_y(h[0], rows[0])) + add[2],
        ]
    )


def local(
    adjoint_electric,
    adjoint_magnetic,
    second_electric,
    second_magnetic,
    saved_forward,
    saved_tangent,
    direction,
    material,
    source_mask,
):
    planes = adjoint_electric.shape[1]
    permittivity = jnp.where(
        material == 0,
        jnp.float32(2.6),
        jnp.where(material == 1, jnp.float32(1.8), jnp.float32(1.0)),
    )
    coefficient = TIME_STEP / permittivity
    slope = -TIME_STEP * direction / (permittivity * permittivity)
    source = source_mask.astype(jnp.float32)
    first_weight = TIME_STEP / (permittivity * permittivity)
    second_weight = 2.0 * TIME_STEP * direction / (permittivity * permittivity * permittivity)

    ea = [adjoint_electric[:, p] for p in range(planes)]
    ha = [adjoint_magnetic[:, p] for p in range(planes)]
    es = [second_electric[:, p] for p in range(planes)]
    hs = [second_magnetic[:, p] for p in range(planes)]
    coef = [coefficient[p] for p in range(planes)]
    slo = [slope[p] for p in range(planes)]
    src = [source[p] for p in range(planes)]
    fw1 = [first_weight[p] for p in range(planes)]
    fw2 = [second_weight[p] for p in range(planes)]
    curvature = [None] * planes

    total_steps = saved_forward.shape[0]
    for section in reversed(range(total_steps)):
      forward = [saved_forward[section][:, p].astype(jnp.float32) for p in range(planes)]
      tangent = [saved_tangent[section][:, p].astype(jnp.float32) for p in range(planes)]
      wa = [coef[p] * ea[p] for p in range(planes)]
      ws = [coef[p] * es[p] + slo[p] * ea[p] for p in range(planes)]
      last = planes - 1
      edge_x = jnp.stack([wa[last][1], wa[last][2], ws[last][1], ws[last][2]])
      before_x = from_behind(edge_x, "gx", 1)
      edge_y = jnp.stack([jnp.stack([wa[p][0, -1], wa[p][2, -1], ws[p][0, -1], ws[p][2, -1]]) for p in range(planes)])
      before_y = from_behind(edge_y, "gy", 1)

      ha_new = [None] * planes
      hs_new = [None] * planes
      edge_d = jnp.stack([wa[0][0, -1], ws[0][0, -1]])
      before_d = lax.ppermute(edge_d, ("gx", "gy"), diagonal_route())
      no_rows = jnp.zeros((2,) + wa[0].shape[2:], wa[0].dtype)
      pa = magnetic_plane(ha[0], wa[0], None, no_rows)
      ps = magnetic_plane(hs[0], ws[0], None, no_rows)
      front_x = lax.optimization_barrier(jnp.stack([pa[1], pa[2], ps[1], ps[2]]))
      after_x = from_behind(front_x, "gx", -1)
      for p in range(1, planes):
          ha_new[p] = magnetic_plane(ha[p], wa[p], wa[p - 1], before_y[p, 0:2])
          hs_new[p] = magnetic_plane(hs[p], ws[p], ws[p - 1], before_y[p, 2:4])
      ha_new[0] = jnp.stack(
          [
              ha[0][0] + TIME_STEP * (back_y(wa[0][2], before_y[0, 1]) - back_z(wa[0][1])),
              front_x[0] + TIME_STEP * before_x[1],
              add_row0(front_x[1] - TIME_STEP * before_x[0], TIME_STEP * before_y[0, 0]),
          ]
      )
      hs_new[0] = jnp.stack(
          [
              hs[0][0] + TIME_STEP * (back_y(ws[0][2], before_y[0, 3]) - back_z(ws[0][1])),
              front_x[2] + TIME_STEP * before_x[3],
              add_row0(front_x[3] - TIME_STEP * before_x[2], TIME_STEP * before_y[0, 2]),
          ]
      )
      ha, hs = lax.optimization_barrier((ha_new, hs_new))
      front_y = jnp.stack([jnp.stack([ha[p][0, 0], ha[p][2, 0], hs[p][0, 0], hs[p][2, 0]]) for p in range(planes)])
      after_y = from_behind(front_y, "gy", -1)
      right_a = jnp.stack(
          [after_x[0] + TIME_STEP * edge_x[1], add_row0(after_x[1] - TIME_STEP * edge_x[0], TIME_STEP * before_d[0])]
      )
      right_s = jnp.stack(
          [after_x[2] + TIME_STEP * edge_x[3], add_row0(after_x[3] - TIME_STEP * edge_x[2], TIME_STEP * before_d[1])]
      )

      ea_new = [None] * planes
      es_new = [None] * planes
      for p in range(planes):
          nxt_a = right_a if p == last else ha[p + 1][1:3]
          nxt_s = right_s if p == last else hs[p + 1][1:3]
          ea_new[p] = electric_plane(ea[p], ha[p], nxt_a, after_y[p, 0:2], src[p] * forward[p])
          es_new[p] = electric_plane(es[p], hs[p], nxt_s, after_y[p, 2:4], src[p] * tangent[p])
      ea, es = ea_new, es_new
      for p in range(planes):
          term = -fw1[p] * jnp.sum(tangent[p] * ea[p] + forward[p] * es[p], axis=0) + fw2[p] * jnp.sum(
              forward[p] * ea[p], axis=0
          )
          curvature[p] = term if curvature[p] is None else curvature[p] + term
    return (
        jnp.stack(curvature),
        jnp.stack(es, axis=1),
        jnp.stack(hs, axis=1),
    )


def solution(mesh):
    in_specs = (
        P(None, "gx", "gy", None),
        P(None, "gx", "gy", None),
        P(None, "gx", "gy", None),
        P(None, "gx", "gy", None),
        P(None, None, "gx", "gy", None),
        P(None, None, "gx", "gy", None),
        P("gx", "gy", None),
        P("gx", "gy", None),
        P("gx", "gy", None),
    )
    out_specs = (P("gx", "gy", None), P(None, "gx", "gy", None), P(None, "gx", "gy", None))
    return jax.shard_map(local, mesh=mesh, in_specs=in_specs, out_specs=out_specs, check_vma=False)
```

```python
import jax
import jax.numpy as jnp
from jax import lax
from jax.sharding import PartitionSpec as P


TIME_STEP = 0.5


def from_behind(block, axis, distance):
    devices = range(lax.axis_size(axis))
    route = [((i - distance) % len(devices), i) for i in devices]
    return lax.ppermute(block, axis, route)


def back_y(f, row):
    return f - jnp.concatenate([row[None], f[:-1]], axis=0)


def back_z(f):
    return f - jnp.pad(f[:, :-1], ((0, 0), (1, 0)))


def ahead_y(f, row):
    return jnp.concatenate([f[1:], row[None]], axis=0) - f


def ahead_z(f):
    return jnp.pad(f[:, 1:], ((0, 0), (0, 1))) - f


def magnetic_plane(h, w, prev, rows):
    bx2 = w[2] if prev is None else w[2] - prev[2]
    bx1 = w[1] if prev is None else w[1] - prev[1]
    return jnp.stack(
        [
            h[0] + TIME_STEP * (back_y(w[2], rows[1]) - back_z(w[1])),
            h[1] + TIME_STEP * (back_z(w[0]) - bx2),
            h[2] + TIME_STEP * (bx1 - back_y(w[0], rows[0])),
        ]
    )


def electric_plane(e, h, nxt, rows, add):
    return jnp.stack(
        [
            e[0] - TIME_STEP * (ahead_y(h[2], rows[1]) - ahead_z(h[1])) + add[0],
            e[1] - TIME_STEP * (ahead_z(h[0]) - (nxt[1] - h[2])) + add[1],
            e[2] - TIME_STEP * ((nxt[0] - h[1]) - ahead_y(h[0], rows[0])) + add[2],
        ]
    )


def local(
    adjoint_electric,
    adjoint_magnetic,
    second_electric,
    second_magnetic,
    saved_forward,
    saved_tangent,
    direction,
    material,
    source_mask,
):
    planes = adjoint_electric.shape[1]
    permittivity = jnp.where(
        material == 0,
        jnp.float32(2.6),
        jnp.where(material == 1, jnp.float32(1.8), jnp.float32(1.0)),
    )
    coefficient = TIME_STEP / permittivity
    slope = -TIME_STEP * direction / (permittivity * permittivity)
    source = source_mask.astype(jnp.float32)
    first_weight = TIME_STEP / (permittivity * permittivity)
    second_weight = 2.0 * TIME_STEP * direction / (permittivity * permittivity * permittivity)

    ea = [adjoint_electric[:, p] for p in range(planes)]
    ha = [adjoint_magnetic[:, p] for p in range(planes)]
    es = [second_electric[:, p] for p in range(planes)]
    hs = [second_magnetic[:, p] for p in range(planes)]
    coef = [coefficient[p] for p in range(planes)]
    slo = [slope[p] for p in range(planes)]
    src = [source[p] for p in range(planes)]
    fw1 = [first_weight[p] for p in range(planes)]
    fw2 = [second_weight[p] for p in range(planes)]
    curvature = [None] * planes

    total_steps = saved_forward.shape[0]
    for section in reversed(range(total_steps)):
      forward = [saved_forward[section][:, p].astype(jnp.float32) for p in range(planes)]
      tangent = [saved_tangent[section][:, p].astype(jnp.float32) for p in range(planes)]
      wa = [coef[p] * ea[p] for p in range(planes)]
      ws = [coef[p] * es[p] + slo[p] * ea[p] for p in range(planes)]
      last = planes - 1
      edge_x = jnp.stack([wa[last][1], wa[last][2], ws[last][1], ws[last][2]])
      before_x = from_behind(edge_x, "gx", 1)
      edge_y = jnp.stack([jnp.stack([wa[p][0, -1], wa[p][2, -1], ws[p][0, -1], ws[p][2, -1]]) for p in range(planes)])
      before_y = from_behind(edge_y, "gy", 1)

      ha_new = [None] * planes
      hs_new = [None] * planes
      ha_new[0] = magnetic_plane(ha[0], wa[0], None, before_y[0, 0:2])
      hs_new[0] = magnetic_plane(hs[0], ws[0], None, before_y[0, 2:4])
      front_x = jnp.stack([ha_new[0][1], ha_new[0][2], hs_new[0][1], hs_new[0][2]])
      ha_new[0], hs_new[0], front_x = lax.optimization_barrier((ha_new[0], hs_new[0], front_x))
      after_x = from_behind(front_x, "gx", -1)
      for p in range(1, planes):
          ha_new[p] = magnetic_plane(ha[p], wa[p], wa[p - 1], before_y[p, 0:2])
          hs_new[p] = magnetic_plane(hs[p], ws[p], ws[p - 1], before_y[p, 2:4])
      ha_new[0] = jnp.stack(
          [ha_new[0][0], ha_new[0][1] + TIME_STEP * before_x[1], ha_new[0][2] - TIME_STEP * before_x[0]]
      )
      hs_new[0] = jnp.stack(
          [hs_new[0][0], hs_new[0][1] + TIME_STEP * before_x[3], hs_new[0][2] - TIME_STEP * before_x[2]]
      )
      ha, hs = lax.optimization_barrier((ha_new, hs_new))
      front_y = jnp.stack([jnp.stack([ha[p][0, 0], ha[p][2, 0], hs[p][0, 0], hs[p][2, 0]]) for p in range(planes)])
      after_y = from_behind(front_y, "gy", -1)
      right_a = jnp.stack([after_x[0] + TIME_STEP * edge_x[1], after_x[1] - TIME_STEP * edge_x[0]])
      right_s = jnp.stack([after_x[2] + TIME_STEP * edge_x[3], after_x[3] - TIME_STEP * edge_x[2]])

      ea_new = [None] * planes
      es_new = [None] * planes
      for p in range(planes):
          nxt_a = right_a if p == last else ha[p + 1][1:3]
          nxt_s = right_s if p == last else hs[p + 1][1:3]
          ea_new[p] = electric_plane(ea[p], ha[p], nxt_a, after_y[p, 0:2], src[p] * forward[p])
          es_new[p] = electric_plane(es[p], hs[p], nxt_s, after_y[p, 2:4], src[p] * tangent[p])
          term = -fw1[p] * jnp.sum(tangent[p] * ea_new[p] + forward[p] * es_new[p], axis=0) + fw2[
              p
          ] * jnp.sum(forward[p] * ea_new[p], axis=0)
          curvature[p] = term if curvature[p] is None else curvature[p] + term
      ea, es = ea_new, es_new
    return (
        jnp.stack(curvature),
        jnp.stack(es, axis=1),
        jnp.stack(hs, axis=1),
    )


def solution(mesh):
    in_specs = (
        P(None, "gx", "gy", None),
        P(None, "gx", "gy", None),
        P(None, "gx", "gy", None),
        P(None, "gx", "gy", None),
        P(None, None, "gx", "gy", None),
        P(None, None, "gx", "gy", None),
        P("gx", "gy", None),
        P("gx", "gy", None),
        P("gx", "gy", None),
    )
    out_specs = (P("gx", "gy", None), P(None, "gx", "gy", None), P(None, "gx", "gy", None))
    return jax.shard_map(local, mesh=mesh, in_specs=in_specs, out_specs=out_specs, check_vma=False)
```
